512 devices in a mesh: section: 8 (over y), peer: 64 (over x, z, core).
Axes of the slice: x: 4, y: 8, z: 8, core: 2. Of those that a mesh axis runs over, the one named last changes fastest.
Arguments:
- inputs: bfloat16 [8192, 2560], P('peer'), may hold values from -6 to 6
- norm_gain: bfloat16 [8, 2560], P('section'), may hold values from 0.099609375 to 1.8984375
- w_down: bfloat16 [8, 64, 192, 2560], P('section', 'peer'), may hold values from -0.125 to 0.125
- w_up: bfloat16 [8, 64, 192, 2560], P('section', 'peer'), may hold values from -0.4375 to 0.4375
- routes: int32 [7, 2, 64, 64], replicated, may hold values from 0 to 63, as said below
- bit_order: int32 [6], replicated, may hold values from 0 to 5, each once
Outputs:
- grad_shards: float32 [8, 983040], P('section', 'peer')
The draws below stay inside these ranges and needn't reach their ends.
Inputs may be any that keep to these rules, and one draw needn't show every extreme that they name: For each boundary s and micro-batch m, the lists routes[s, m, p, :] of all replicas p hold the same 64 distinct lanes, each list in its own order. `bit_order`: each bit number appears once.
All inputs are finite; a program needn't handle non-finite values.
Results may differ from the reference program's by a relative error of at most 0.023.
Values may be sent and summed in bfloat16 or wider, within the bound.
No kernel may reach another device: no remote copies, remote signals or barrier semaphores. Data moves between devices by JAX's collectives and lax.ppermute only.
A program may use at most 128 MiB of HBM per device.

```python
from functools import partial
import jax
import jax.numpy as jnp
from jax import lax

D = 2560
BOTTLENECK = 192
MICRO = 2
BATCH_ROWS = 64
LANES = 64
PEER_BITS = 6
ROWS_ALL = 8192
SHARD = 15360
N_SECTION = 8
N_PEER = 64


def boundary_lanes(key):
    lane_key, order_key = jax.random.split(key)
    forced = jnp.array([0, 1, N_PEER // 2, LANES - 1], jnp.int32)
    lane_ids = jnp.arange(LANES, dtype=jnp.int32)
    is_forced = jnp.any(lane_ids[:, None] == forced[None, :], axis=1).astype(jnp.int32)
    ranks = jax.random.permutation(lane_key, LANES).astype(jnp.int32)
    scores = ranks + LANES * is_forced
    middle = jnp.argsort(scores)[:BATCH_ROWS - 4].astype(jnp.int32)
    used_lanes = jnp.concatenate([forced, middle])
    peer_keys = jax.random.split(order_key, N_PEER)
    orders = jax.vmap(lambda member: jax.random.permutation(member, BATCH_ROWS))(peer_keys)
    return used_lanes[orders]


def draw_routes(key, part):
    section_keys = jax.random.split(jax.random.fold_in(key, 11), (N_SECTION - 1) * MICRO)
    lanes = jax.vmap(boundary_lanes)(section_keys).astype(jnp.int32)
    return lanes.reshape(N_SECTION - 1, MICRO, N_PEER, BATCH_ROWS)


def block_scale(key, shape, shards, least, largest):
    gain = 1.0
    for axis_at, shards_of in shards:
        draws = jax.random.uniform(jax.random.fold_in(jax.random.fold_in(key, 6), axis_at), (shards_of,), jnp.float32, least / len(shards), largest / len(shards))
        gain = gain * jnp.repeat(jnp.exp(draws), shape[axis_at] // shards_of).reshape((-1,) + (1,) * (len(shape) - 1 - axis_at))
    return gain


def bell_draw(rng, dims, scale, reach, shards=(), kind=jnp.bfloat16):
    gain = block_scale(rng, dims, shards, -0.22, 0.18) if shards else 1.0
    values = jax.random.normal(rng, dims, jnp.float32) * scale * gain
    return jnp.minimum(jnp.maximum(values, -reach), reach).astype(kind)


def setup_inputs(seed: int = 0) -> dict:
    arg_keys = jax.random.split(jax.random.key(seed), 7)
    inputs = bell_draw(arg_keys[0], (ROWS_ALL, D), 1.0, 6.0, ((0, 64),))
    norm_gain = jnp.clip(1.0 + 0.18 * jax.random.normal(arg_keys[1], (N_SECTION, D), jnp.float32), 0.099609375, 1.8984375).astype(jnp.bfloat16)
    w_down = bell_draw(arg_keys[2], (N_SECTION, N_PEER, BOTTLENECK, D), D ** -0.5, 0.125, ((0, 8), (1, 64)))
    w_up = bell_draw(arg_keys[3], (N_SECTION, N_PEER, BOTTLENECK, D), BOTTLENECK ** -0.5, 0.4375, ((0, 8), (1, 64)))
    routes = draw_routes(jax.random.fold_in(arg_keys[6], 71), 0)
    bit_order = jax.random.permutation(arg_keys[5], PEER_BITS).astype(jnp.int32)
    return dict(inputs=inputs, norm_gain=norm_gain, w_down=w_down, w_up=w_up, routes=routes, bit_order=bit_order)


gelu_scale = 0.7978845608028654
gelu_cubic = 0.044715
norm_eps = 1e-05

def gelu_parts(hidden):
    tangent = jnp.tanh(gelu_scale * (hidden + gelu_cubic * hidden * hidden * hidden))
    gelu_value = 0.5 * hidden * (1.0 + tangent)
    gelu_slope = 0.5 * (1.0 + tangent) + 0.5 * hidden * (1.0 - tangent * tangent) * gelu_scale * (1.0 + 3.0 * gelu_cubic * hidden * hidden)
    return (gelu_value, gelu_slope)

def normalize(row_block, gain_row):
    x_float = row_block.astype(jnp.float32)
    inv_rms = lax.rsqrt(lax.optimization_barrier(jnp.mean(x_float * x_float, axis=-1, keepdims=True)) + norm_eps)
    normed = (x_float * inv_rms * gain_row.astype(jnp.float32)).astype(jnp.bfloat16)
    return (x_float, inv_rms, normed)

def contract_last(left, right):
    return lax.dot_general(left, right, (((1,), (1,)), ((), ())), preferred_element_type=jnp.float32)

def contract_first(left, right):
    return lax.dot_general(left, right, (((0,), (0,)), ((), ())), preferred_element_type=jnp.float32)

def forward_member(gain_row, member):
    row_block, down_proj, up_proj = member
    x_float, inv_rms, normed = normalize(row_block, gain_row)
    hidden = contract_last(normed, down_proj)
    gelu_value, gelu_slope = gelu_parts(hidden)
    active = gelu_value.astype(jnp.bfloat16)
    return (x_float + jnp.dot(active, up_proj, preferred_element_type=jnp.float32)).astype(jnp.bfloat16)

def backward_member(gain_row, member):
    row_block, upstream, down_proj, up_proj = member
    x_float, inv_rms, normed = normalize(row_block, gain_row)
    hidden = contract_last(normed, down_proj)
    gelu_value, gelu_slope = gelu_parts(hidden)
    active = gelu_value.astype(jnp.bfloat16)
    grad_up = contract_first(active, upstream)
    grad_active = contract_last(upstream, up_proj)
    grad_hidden = (grad_active * gelu_slope).astype(jnp.bfloat16)
    grad_down = contract_first(grad_hidden, normed)
    grad_normed = jnp.dot(grad_hidden, down_proj, preferred_element_type=jnp.float32) * gain_row.astype(jnp.float32)
    inner_term = lax.optimization_barrier(jnp.mean(grad_normed * x_float, axis=-1, keepdims=True))
    grad_rows = (upstream.astype(jnp.float32) + inv_rms * (grad_normed - x_float * inv_rms * inv_rms * inner_term)).astype(jnp.bfloat16)
    return (grad_rows, grad_down, grad_up)

def route_indices(lane_ids):
    used_lanes = jnp.sort(lane_ids[0])
    peer_ids = jnp.arange(N_PEER, dtype=jnp.int32)
    slot_ids = jnp.broadcast_to(jnp.arange(BATCH_ROWS, dtype=jnp.int32)[None, :], (N_PEER, BATCH_ROWS))
    inverse = jnp.zeros((N_PEER, LANES), jnp.int32).at[peer_ids[:, None], lane_ids].set(slot_ids)
    sources = ((peer_ids[:, None] - used_lanes[None, :] % N_PEER) % N_PEER).astype(jnp.int32)
    source_slots = inverse[sources, jnp.broadcast_to(used_lanes[None, :], (N_PEER, BATCH_ROWS))]
    return (sources, source_slots)

def shard_ids(bit_order):
    peer_ids = jnp.arange(N_PEER, dtype=jnp.int32)
    bit_table = jnp.right_shift(peer_ids[:, None], bit_order[None, :]) & 1
    weights = jnp.left_shift(jnp.int32(1), PEER_BITS - 1 - jnp.arange(PEER_BITS, dtype=jnp.int32))
    return lax.optimization_barrier(jnp.sum(bit_table * weights[None, :], axis=1)).astype(jnp.int32)

def reference(inputs, norm_gain, w_down, w_up, routes, bit_order):
    all_rows = inputs.reshape(N_PEER, MICRO, BATCH_ROWS, D)
    totals = [jnp.zeros((2 * BOTTLENECK * D,), jnp.float32) for s in range(N_SECTION)]
    for m in range(MICRO):
        section_rows = all_rows[:, m]
        saved_rows = []
        outputs = section_rows
        for s in range(N_SECTION):
            saved_rows.append(section_rows)
            outputs = lax.map(partial(forward_member, norm_gain[s]), (section_rows, w_down[s], w_up[s]))
            if s < N_SECTION - 1:
                sources, source_slots = route_indices(routes[s, m])
                section_rows = outputs[sources, source_slots]
        upstream = outputs
        for s in reversed(range(N_SECTION)):
            grad_rows, grad_down, grad_up = lax.map(partial(backward_member, norm_gain[s]), (saved_rows[s], upstream, w_down[s], w_up[s]))
            summed = jnp.concatenate([lax.optimization_barrier(jnp.sum(grad_down, axis=0)).reshape(-1), lax.optimization_barrier(jnp.sum(grad_up, axis=0)).reshape(-1)])
            totals[s] = totals[s] + summed
            if s > 0:
                sources, source_slots = route_indices(routes[s - 1, m])
                upstream = jnp.zeros_like(grad_rows).at[sources, source_slots].set(grad_rows)
    shard_order = shard_ids(bit_order)
    results = []
    for s in range(N_SECTION):
        averaged = totals[s] * (1.0 / N_PEER)
        results.append(averaged.reshape(N_PEER, SHARD)[shard_order].reshape(-1))
    return jnp.stack(results)
```

```python
import jax
import jax.numpy as jnp
from jax import lax
from jax.sharding import PartitionSpec as P

gelu_scale = 0.7978845608028654
gelu_cubic = 0.044715
norm_eps = 1e-05


def gelu_parts(hidden):
    tangent = jnp.tanh(gelu_scale * (hidden + gelu_cubic * hidden * hidden * hidden))
    gelu_value = 0.5 * hidden * (1.0 + tangent)
    gelu_slope = 0.5 * (1.0 + tangent) + 0.5 * hidden * (1.0 - tangent * tangent) * gelu_scale * (
        1.0 + 3.0 * gelu_cubic * hidden * hidden
    )
    return (gelu_value, gelu_slope)


def normalize(row_block, gain_row):
    x_float = row_block.astype(jnp.float32)
    inv_rms = lax.rsqrt(jnp.mean(x_float * x_float, axis=-1, keepdims=True) + norm_eps)
    normed = (x_float * inv_rms * gain_row.astype(jnp.float32)).astype(jnp.bfloat16)
    return (x_float, inv_rms, normed)


def contract_last(left, right):
    return lax.dot_general(
        left, right, (((1,), (1,)), ((), ())), preferred_element_type=jnp.float32
    )


def contract_first(left, right):
    return lax.dot_general(
        left, right, (((0,), (0,)), ((), ())), preferred_element_type=jnp.float32
    )


def permute_rows(onehot, rows, spec):
    return jnp.einsum(spec, onehot, rows, preferred_element_type=jnp.float32).astype(rows.dtype)


def local(inputs, norm_gain, w_down, w_up, routes, bit_order):
    sections = lax.axis_size("section")
    peer_count = lax.axis_size("peer")
    section_now = lax.axis_index("section")
    peer_now = lax.axis_index("peer")
    down_proj = w_down[0, 0]
    up_proj = w_up[0, 0]
    gain_row = norm_gain[0]
    gain_float = gain_row.astype(jnp.float32)
    micro_count = routes.shape[1]
    batch_rows = routes.shape[3]
    feature_count = inputs.shape[1]
    row_count = micro_count * batch_rows

    slots = jnp.arange(batch_rows, dtype=jnp.int32)
    own_lanes = routes[:, :, peer_now, :]
    arrived_rows = (peer_now - slots) % batch_rows
    slot_lanes = jnp.concatenate(
        [own_lanes[:1], jnp.take(own_lanes[1:], arrived_rows, axis=2)], axis=0
    )
    destinations = (peer_now + slot_lanes) % peer_count
    send_onehot = (
        destinations[:, :, None, :] == jnp.arange(peer_count, dtype=jnp.int32)[None, None, :, None]
    ).astype(jnp.bfloat16)

    x = inputs.reshape(micro_count, batch_rows, feature_count)
    keep_x = jnp.zeros((row_count, feature_count), jnp.bfloat16)
    keep_inv = jnp.zeros((row_count, 1), jnp.float32)
    keep_normed = jnp.zeros((row_count, feature_count), jnp.bfloat16)
    keep_active = jnp.zeros((row_count, down_proj.shape[0]), jnp.bfloat16)
    keep_slope = jnp.zeros((row_count, down_proj.shape[0]), jnp.float32)
    upstream = None
    for k in range(sections):
        flat = x.reshape(row_count, feature_count)
        x_float, inv_rms, normed = normalize(flat, gain_row)
        hidden = contract_last(normed, down_proj)
        gelu_value, gelu_slope = gelu_parts(hidden)
        active = gelu_value.astype(jnp.bfloat16)
        outputs = (x_float + jnp.dot(active, up_proj, preferred_element_type=jnp.float32)).astype(
            jnp.bfloat16
        )
        mine = section_now == k
        keep_x = jnp.where(mine, flat, keep_x)
        keep_inv = jnp.where(mine, inv_rms, keep_inv)
        keep_normed = jnp.where(mine, normed, keep_normed)
        keep_active = jnp.where(mine, active, keep_active)
        keep_slope = jnp.where(mine, gelu_slope, keep_slope)
        if k < sections - 1:
            packed = permute_rows(
                send_onehot[k], outputs.reshape(micro_count, batch_rows, feature_count), "mdq,mqf->mdf"
            )
            received = lax.all_to_all(packed, "peer", 1, 1, tiled=True)
            x = lax.ppermute(received, "section", [(k, k + 1)])
        else:
            upstream = outputs

    x_float = keep_x.astype(jnp.float32)
    keep_upstream = jnp.zeros((row_count, feature_count), jnp.bfloat16)
    keep_grad_hidden = jnp.zeros((row_count, down_proj.shape[0]), jnp.bfloat16)
    for k in reversed(range(sections)):
        grad_active = contract_last(upstream, up_proj)
        grad_hidden = (grad_active * keep_slope).astype(jnp.bfloat16)
        grad_normed = jnp.dot(grad_hidden, down_proj, preferred_element_type=jnp.float32) * gain_float
        inner_term = jnp.mean(grad_normed * x_float, axis=-1, keepdims=True)
        grad_rows = (
            upstream.astype(jnp.float32)
            + keep_inv * (grad_normed - x_float * keep_inv * keep_inv * inner_term)
        ).astype(jnp.bfloat16)
        mine = section_now == k
        keep_upstream = jnp.where(mine, upstream, keep_upstream)
        keep_grad_hidden = jnp.where(mine, grad_hidden, keep_grad_hidden)
        if k > 0:
            sent = lax.all_to_all(
                grad_rows.reshape(micro_count, batch_rows, feature_count), "peer", 1, 1, tiled=True
            )
            moved = lax.ppermute(sent, "section", [(k, k - 1)])
            upstream = permute_rows(send_onehot[k - 1], moved, "mdq,mdf->mqf").reshape(
                row_count, feature_count
            )

    sum_down = contract_first(keep_grad_hidden, keep_normed)
    sum_up = contract_first(keep_active, keep_upstream)
    gradient = jnp.concatenate([sum_down.reshape(-1), sum_up.reshape(-1)]).reshape(peer_count, -1)
    bits_count = peer_count.bit_length() - 1
    peers = jnp.arange(peer_count, dtype=jnp.int32)
    bit_table = jnp.right_shift(peers[:, None], bit_order[None, :]) & 1
    weights = jnp.left_shift(jnp.int32(1), bits_count - 1 - jnp.arange(bits_count, dtype=jnp.int32))
    shard_of = jnp.sum(bit_table * weights[None, :], axis=1).astype(jnp.int32)
    ordered = jnp.take(gradient, shard_of, axis=0)
    shard = lax.psum_scatter(ordered, "peer", scatter_dimension=0, tiled=True)
    return (shard * (1.0 / peer_count)).reshape(1, -1)


def solution(mesh):
    placed = (
        P("peer", None),
        P("section", None),
        P("section", "peer", None, None),
        P("section", "peer", None, None),
        P(),
        P(),
    )
    return jax.shard_map(
        local, mesh=mesh, in_specs=placed, out_specs=P("section", "peer"), check_vma=False
    )
```

```python
import jax
import jax.numpy as jnp
from jax import lax
from jax.sharding import PartitionSpec as P

gelu_scale = 0.7978845608028654
gelu_cubic = 0.044715
norm_eps = 1e-05


def gelu_parts(hidden):
    tangent = jnp.tanh(gelu_scale * (hidden + gelu_cubic * hidden * hidden * hidden))
    gelu_value = 0.5 * hidden * (1.0 + tangent)
    gelu_slope = 0.5 * (1.0 + tangent) + 0.5 * hidden * (1.0 - tangent * tangent) * gelu_scale * (
        1.0 + 3.0 * gelu_cubic * hidden * hidden
    )
    return (gelu_value, gelu_slope)


def normalize(row_block, gain_row):
    x_float = row_block.astype(jnp.float32)
    inv_rms = lax.rsqrt(jnp.mean(x_float * x_float, axis=-1, keepdims=True) + norm_eps)
    normed = (x_float * inv_rms * gain_row.astype(jnp.float32)).astype(jnp.bfloat16)
    return (x_float, inv_rms, normed)


def contract_last(left, right):
    return lax.dot_general(
        left, right, (((1,), (1,)), ((), ())), preferred_element_type=jnp.float32
    )


def contract_first(left, right):
    return lax.dot_general(
        left, right, (((0,), (0,)), ((), ())), preferred_element_type=jnp.float32
    )


def permute_rows(onehot, rows, spec):
    return jnp.einsum(spec, onehot, rows, preferred_element_type=jnp.float32).astype(rows.dtype)


def local(inputs, norm_gain, w_down, w_up, routes, bit_order):
    sections = lax.axis_size("section")
    peer_count = lax.axis_size("peer")
    section_now = lax.axis_index("section")
    peer_now = lax.axis_index("peer")
    down_proj = w_down[0, 0]
    up_proj = w_up[0, 0]
    gain_row = norm_gain[0]
    gain_float = gain_row.astype(jnp.float32)
    micro_count = routes.shape[1]
    batch_rows = routes.shape[3]
    feature_count = inputs.shape[1]
    row_count = micro_count * batch_rows

    slots = jnp.arange(batch_rows, dtype=jnp.int32)
    own_lanes = routes[:, :, peer_now, :]
    arrived_rows = (peer_now - slots) % batch_rows
    slot_lanes = jnp.concatenate(
        [own_lanes[:1], jnp.take(own_lanes[1:], arrived_rows, axis=2)], axis=0
    )
    destinations = (peer_now + slot_lanes) % peer_count
    send_onehot = (
        destinations[:, :, None, :] == jnp.arange(peer_count, dtype=jnp.int32)[None, None, :, None]
    ).astype(jnp.bfloat16)

    x = inputs.reshape(micro_count, batch_rows, feature_count)
    keep_x = jnp.zeros((row_count, feature_count), jnp.bfloat16)
    keep_inv = jnp.zeros((row_count, 1), jnp.float32)
    keep_normed = jnp.zeros((row_count, feature_count), jnp.bfloat16)
    keep_active = jnp.zeros((row_count, down_proj.shape[0]), jnp.bfloat16)
    keep_slope = jnp.zeros((row_count, down_proj.shape[0]), jnp.float32)
    upstream = None
    for k in range(sections):
        flat = x.reshape(row_count, feature_count)
        x_float, inv_rms, normed = normalize(flat, gain_row)
        hidden = contract_last(normed, down_proj)
        gelu_value, gelu_slope = gelu_parts(hidden)
        active = gelu_value.astype(jnp.bfloat16)
        outputs = (x_float + jnp.dot(active, up_proj, preferred_element_type=jnp.float32)).astype(
            jnp.bfloat16
        )
        mine = section_now == k
        keep_x = jnp.where(mine, flat, keep_x)
        keep_inv = jnp.where(mine, inv_rms, keep_inv)
        keep_normed = jnp.where(mine, normed, keep_normed)
        keep_active = jnp.where(mine, active, keep_active)
        keep_slope = jnp.where(mine, gelu_slope, keep_slope)
        if k < sections - 1:
            packed = permute_rows(
                send_onehot[k], outputs.reshape(micro_count, batch_rows, feature_count), "mdq,mqf->mdf"
            )
            received = lax.all_to_all(packed, "peer", 1, 1, tiled=True)
            x = lax.ppermute(received, "section", [(k, k + 1)])
        else:
            upstream = outputs

    x_float = keep_x.astype(jnp.float32)
    keep_upstream = jnp.zeros((row_count, feature_count), jnp.bfloat16)
    keep_grad_hidden = jnp.zeros((row_count, down_proj.shape[0]), jnp.bfloat16)
    for k in reversed(range(sections)):
        grad_active = contract_last(upstream, up_proj)
        grad_hidden = (grad_active * keep_slope).astype(jnp.bfloat16)
        grad_normed = jnp.dot(grad_hidden, down_proj, preferred_element_type=jnp.float32) * gain_float
        inner_term = jnp.mean(grad_normed * x_float, axis=-1, keepdims=True)
        grad_rows = (
            upstream.astype(jnp.float32)
            + keep_inv * (grad_normed - x_float * keep_inv * keep_inv * inner_term)
        ).astype(jnp.bfloat16)
        mine = section_now == k
        keep_upstream = jnp.where(mine, upstream, keep_upstream)
        keep_grad_hidden = jnp.where(mine, grad_hidden, keep_grad_hidden)
        if k > 0:
            sent = lax.all_to_all(
                grad_rows.reshape(micro_count, batch_rows, feature_count), "peer", 1, 1, tiled=True
            )
            moved = lax.ppermute(sent, "section", [(k, k - 1)])
            upstream = permute_rows(send_onehot[k - 1], moved, "mdq,mdf->mqf").reshape(
                row_count, feature_count
            )

    bits_count = peer_count.bit_length() - 1
    peers = jnp.arange(peer_count, dtype=jnp.int32)
    halving_bits = [0, 1, 4, 2, 5, 3][:bits_count]
    position_peer = jnp.zeros((peer_count,), jnp.int32)
    for t, b in enumerate(halving_bits):
        position_peer = position_peer + (((peers >> (bits_count - 1 - t)) & 1) << b)
    bit_table = jnp.right_shift(position_peer[:, None], bit_order[None, :]) & 1
    weights = jnp.left_shift(jnp.int32(1), bits_count - 1 - jnp.arange(bits_count, dtype=jnp.int32))
    source_chunk = jnp.sum(bit_table * weights[None, :], axis=1).astype(jnp.int32)
    units = down_proj.shape[0]
    chunk_rows = 2 * units // peer_count
    column_source = (
        source_chunk[:, None] * chunk_rows + jnp.arange(chunk_rows, dtype=jnp.int32)[None, :]
    ).reshape(-1)
    left = jnp.zeros((2 * row_count, 2 * units), jnp.bfloat16)
    left = left.at[:row_count, :units].set(keep_grad_hidden).at[row_count:, units:].set(keep_active)
    left = jnp.take(left, column_source, axis=1)
    right = jnp.concatenate([keep_normed, keep_upstream], axis=0)
    current = contract_first(left, right).reshape(-1)
    for b in halving_bits:
        own_bit = (peer_now >> b) & 1
        half_len = current.shape[0] // 2
        outgoing = lax.dynamic_slice(current, ((1 - own_bit) * half_len,), (half_len,))
        kept = lax.dynamic_slice(current, (own_bit * half_len,), (half_len,))
        mask = 2**b
        pairs = [(source, source ^ mask) for source in range(peer_count)]
        current = kept + lax.ppermute(outgoing, "peer", pairs)
    return (current * (1.0 / peer_count)).reshape(1, -1)


def solution(mesh):
    placed = (
        P("peer", None),
        P("section", None),
        P("section", "peer", None, None),
        P("section", "peer", None, None),
        P(),
        P(),
    )
    return jax.shard_map(
        local, mesh=mesh, in_specs=placed, out_specs=P("section", "peer"), check_vma=False
    )
```

```python
import jax
import jax.numpy as jnp
from jax import lax
from jax.sharding import PartitionSpec as P

gelu_scale = 0.7978845608028654
gelu_cubic = 0.044715
norm_eps = 1e-05


def gelu_parts(hidden):
    tangent = jnp.tanh(gelu_scale * (hidden + gelu_cubic * hidden * hidden * hidden))
    gelu_value = 0.5 * hidden * (1.0 + tangent)
    gelu_slope = 0.5 * (1.0 + tangent) + 0.5 * hidden * (1.0 - tangent * tangent) * gelu_scale * (
        1.0 + 3.0 * gelu_cubic * hidden * hidden
    )
    return (gelu_value, gelu_slope)


def normalize(row_block, gain_row):
    x_float = row_block.astype(jnp.float32)
    inv_rms = lax.rsqrt(jnp.mean(x_float * x_float, axis=-1, keepdims=True) + norm_eps)
    normed = (x_float * inv_rms * gain_row.astype(jnp.float32)).astype(jnp.bfloat16)
    return (x_float, inv_rms, normed)


def contract_last(left, right):
    return lax.dot_general(
        left, right, (((1,), (1,)), ((), ())), preferred_element_type=jnp.float32
    )


def contract_first(left, right):
    return lax.dot_general(
        left, right, (((0,), (0,)), ((), ())), preferred_element_type=jnp.float32
    )


def permute_rows(onehot, rows, spec):
    return jnp.einsum(spec, onehot, rows, preferred_element_type=jnp.float32).astype(rows.dtype)


def local(inputs, norm_gain, w_down, w_up, routes, bit_order):
    sections = lax.axis_size("section")
    peer_count = lax.axis_size("peer")
    section_now = lax.axis_index("section")
    peer_now = lax.axis_index("peer")
    down_proj = w_down[0, 0]
    up_proj = w_up[0, 0]
    gain_row = norm_gain[0]
    gain_float = gain_row.astype(jnp.float32)
    micro_count = routes.shape[1]
    batch_rows = routes.shape[3]
    feature_count = inputs.shape[1]
    row_count = micro_count * batch_rows

    slots = jnp.arange(batch_rows, dtype=jnp.int32)
    own_lanes = routes[:, :, peer_now, :]
    arrived_rows = (peer_now - slots) % batch_rows
    slot_lanes = jnp.concatenate(
        [own_lanes[:1], jnp.take(own_lanes[1:], arrived_rows, axis=2)], axis=0
    )
    destinations = (peer_now + slot_lanes) % peer_count
    send_onehot = (
        destinations[:, :, None, :] == jnp.arange(peer_count, dtype=jnp.int32)[None, None, :, None]
    ).astype(jnp.bfloat16)

    x = inputs.reshape(micro_count, batch_rows, feature_count)
    keep_x = jnp.zeros((row_count, feature_count), jnp.bfloat16)
    keep_inv = jnp.zeros((row_count, 1), jnp.float32)
    keep_normed = jnp.zeros((row_count, feature_count), jnp.bfloat16)
    keep_active = jnp.zeros((row_count, down_proj.shape[0]), jnp.bfloat16)
    keep_slope = jnp.zeros((row_count, down_proj.shape[0]), jnp.float32)
    upstream = None
    for k in range(sections):
        flat = x.reshape(row_count, feature_count)
        x_float, inv_rms, normed = normalize(flat, gain_row)
        hidden = contract_last(normed, down_proj)
        gelu_value, gelu_slope = gelu_parts(hidden)
        active = gelu_value.astype(jnp.bfloat16)
        outputs = (x_float + jnp.dot(active, up_proj, preferred_element_type=jnp.float32)).astype(
            jnp.bfloat16
        )
        mine = section_now == k
        keep_x = jnp.where(mine, flat, keep_x)
        keep_inv = jnp.where(mine, inv_rms, keep_inv)
        keep_normed = jnp.where(mine, normed, keep_normed)
        keep_active = jnp.where(mine, active, keep_active)
        keep_slope = jnp.where(mine, gelu_slope, keep_slope)
        if k < sections - 1:
            packed = permute_rows(
                send_onehot[k], outputs.reshape(micro_count, batch_rows, feature_count), "mdq,mqf->mdf"
            )
            received = lax.all_to_all(packed, "peer", 1, 1, tiled=True)
            x = lax.ppermute(received, "section", [(k, k + 1)])
        else:
            upstream = outputs

    x_float = keep_x.astype(jnp.float32)
    keep_upstream = jnp.zeros((row_count, feature_count), jnp.bfloat16)
    keep_grad_hidden = jnp.zeros((row_count, down_proj.shape[0]), jnp.bfloat16)
    for k in reversed(range(sections)):
        grad_active = contract_last(upstream, up_proj)
        grad_hidden = (grad_active * keep_slope).astype(jnp.bfloat16)
        grad_normed = jnp.dot(grad_hidden, down_proj, preferred_element_type=jnp.float32) * gain_float
        inner_term = jnp.mean(grad_normed * x_float, axis=-1, keepdims=True)
        grad_rows = (
            upstream.astype(jnp.float32)
            + keep_inv * (grad_normed - x_float * keep_inv * keep_inv * inner_term)
        ).astype(jnp.bfloat16)
        mine = section_now == k
        keep_upstream = jnp.where(mine, upstream, keep_upstream)
        keep_grad_hidden = jnp.where(mine, grad_hidden, keep_grad_hidden)
        if k > 0:
            sent = lax.all_to_all(
                grad_rows.reshape(micro_count, batch_rows, feature_count), "peer", 1, 1, tiled=True
            )
            moved = lax.ppermute(sent, "section", [(k, k - 1)])
            upstream = permute_rows(send_onehot[k - 1], moved, "mdq,mdf->mqf").reshape(
                row_count, feature_count
            )

    bits_count = peer_count.bit_length() - 1
    peers = jnp.arange(peer_count, dtype=jnp.int32)
    order_even = [1, 4, 2, 5, 3][: bits_count - 1]
    order_odd = [4, 1, 5, 2, 3][: bits_count - 1]
    position_core = peers >> (bits_count - 1)
    position_peer = position_core
    for t in range(bits_count - 1):
        chosen = jnp.where(position_core == 0, order_even[t], order_odd[t])
        position_peer = position_peer + (((peers >> (bits_count - 2 - t)) & 1) << chosen)
    bit_table = jnp.right_shift(position_peer[:, None], bit_order[None, :]) & 1
    weights = jnp.left_shift(jnp.int32(1), bits_count - 1 - jnp.arange(bits_count, dtype=jnp.int32))
    source_chunk = jnp.sum(bit_table * weights[None, :], axis=1).astype(jnp.int32)
    units = down_proj.shape[0]
    chunk_rows = 2 * units // peer_count
    column_source = (
        source_chunk[:, None] * chunk_rows + jnp.arange(chunk_rows, dtype=jnp.int32)[None, :]
    ).reshape(-1)
    left = jnp.zeros((2 * row_count, 2 * units), jnp.bfloat16)
    left = left.at[:row_count, :units].set(keep_grad_hidden).at[row_count:, units:].set(keep_active)
    left = jnp.take(left, column_source, axis=1)
    right = jnp.concatenate([keep_normed, keep_upstream], axis=0)
    current = contract_first(left, right)
    core_now = peer_now & 1
    stage_bits = [(0, 0)] + list(zip(order_even, order_odd))
    for even_bit, odd_bit in stage_bits:
        bit_now = jnp.where(core_now == 0, even_bit, odd_bit)
        own_bit = (peer_now >> bit_now) & 1
        half_len = current.shape[0] // 2
        outgoing = lax.dynamic_slice_in_dim(current, (1 - own_bit) * half_len, half_len, axis=0)
        kept = lax.dynamic_slice_in_dim(current, own_bit * half_len, half_len, axis=0)
        pairs = [
            (source, source ^ (1 << (even_bit if source % 2 == 0 else odd_bit)))
            for source in range(peer_count)
        ]
        current = kept + lax.ppermute(outgoing, "peer", pairs)
    return (current * (1.0 / peer_count)).reshape(1, -1)


def solution(mesh):
    placed = (
        P("peer", None),
        P("section", None),
        P("section", "peer", None, None),
        P("section", "peer", None, None),
        P(),
        P(),
    )
    return jax.shard_map(
        local, mesh=mesh, in_specs=placed, out_specs=P("section", "peer"), check_vma=False
    )
```

```python
import jax
import jax.numpy as jnp
from jax import lax
from jax.sharding import PartitionSpec as P

gelu_scale = 0.7978845608028654
gelu_cubic = 0.044715
norm_eps = 1e-05


def gelu_parts(hidden):
    tangent = jnp.tanh(gelu_scale * (hidden + gelu_cubic * hidden * hidden * hidden))
    gelu_value = 0.5 * hidden * (1.0 + tangent)
    gelu_slope = 0.5 * (1.0 + tangent) + 0.5 * hidden * (1.0 - tangent * tangent) * gelu_scale * (
        1.0 + 3.0 * gelu_cubic * hidden * hidden
    )
    return (gelu_value, gelu_slope)


def normalize(row_block, gain_row):
    x_float = row_block.astype(jnp.float32)
    inv_rms = lax.rsqrt(jnp.mean(x_float * x_float, axis=-1, keepdims=True) + norm_eps)
    normed = (x_float * inv_rms * gain_row.astype(jnp.float32)).astype(jnp.bfloat16)
    return (x_float, inv_rms, normed)


def contract_last(left, right):
    return lax.dot_general(
        left, right, (((1,), (1,)), ((), ())), preferred_element_type=jnp.float32
    )


def contract_first(left, right):
    return lax.dot_general(
        left, right, (((0,), (0,)), ((), ())), preferred_element_type=jnp.float32
    )


def permute_rows(onehot, rows, spec):
    return jnp.einsum(spec, onehot, rows, preferred_element_type=jnp.float32).astype(rows.dtype)


def local(inputs, norm_gain, w_down, w_up, routes, bit_order):
    sections = lax.axis_size("section")
    peer_count = lax.axis_size("peer")
    section_now = lax.axis_index("section")
    peer_now = lax.axis_index("peer")
    down_proj = w_down[0, 0]
    up_proj = w_up[0, 0]
    gain_row = norm_gain[0]
    gain_float = gain_row.astype(jnp.float32)
    micro_count = routes.shape[1]
    batch_rows = routes.shape[3]
    feature_count = inputs.shape[1]
    row_count = micro_count * batch_rows

    slots = jnp.arange(batch_rows, dtype=jnp.int32)
    own_lanes = routes[:, :, peer_now, :]
    arrived_rows = (peer_now - slots) % batch_rows
    slot_lanes = jnp.concatenate(
        [own_lanes[:1], jnp.take(own_lanes[1:], arrived_rows, axis=2)], axis=0
    )
    destinations = (peer_now + slot_lanes) % peer_count
    send_onehot = (
        destinations[:, :, None, :] == jnp.arange(peer_count, dtype=jnp.int32)[None, None, :, None]
    ).astype(jnp.bfloat16)

    x = inputs.reshape(micro_count, batch_rows, feature_count)
    keep_x = jnp.zeros((row_count, feature_count), jnp.bfloat16)
    keep_inv = jnp.zeros((row_count, 1), jnp.float32)
    keep_normed = jnp.zeros((row_count, feature_count), jnp.bfloat16)
    keep_active = jnp.zeros((row_count, down_proj.shape[0]), jnp.bfloat16)
    keep_slope = jnp.zeros((row_count, down_proj.shape[0]), jnp.float32)
    upstream = None
    for k in range(sections):
        flat = x.reshape(row_count, feature_count)
        x_float, inv_rms, normed = normalize(flat, gain_row)
        hidden = contract_last(normed, down_proj)
        gelu_value, gelu_slope = gelu_parts(hidden)
        active = gelu_value.astype(jnp.bfloat16)
        outputs = (x_float + jnp.dot(active, up_proj, preferred_element_type=jnp.float32)).astype(
            jnp.bfloat16
        )
        mine = section_now == k
        keep_x = jnp.where(mine, flat, keep_x)
        keep_inv = jnp.where(mine, inv_rms, keep_inv)
        keep_normed = jnp.where(mine, normed, keep_normed)
        keep_active = jnp.where(mine, active, keep_active)
        keep_slope = jnp.where(mine, gelu_slope, keep_slope)
        if k < sections - 1:
            packed = permute_rows(
                send_onehot[k], outputs.reshape(micro_count, batch_rows, feature_count), "mdq,mqf->mdf"
            )
            received = lax.all_to_all(packed, "peer", 1, 1, tiled=True)
            x = lax.ppermute(received, "section", [(k, k + 1)])
        else:
            upstream = outputs

    x_float = keep_x.astype(jnp.float32)
    keep_upstream = jnp.zeros((row_count, feature_count), jnp.bfloat16)
    keep_grad_hidden = jnp.zeros((row_count, down_proj.shape[0]), jnp.bfloat16)
    for k in reversed(range(sections)):
        grad_active = contract_last(upstream, up_proj)
        grad_hidden = (grad_active * keep_slope).astype(jnp.bfloat16)
        grad_normed = jnp.dot(grad_hidden, down_proj, preferred_element_type=jnp.float32) * gain_float
        inner_term = jnp.mean(grad_normed * x_float, axis=-1, keepdims=True)
        grad_rows = (
            upstream.astype(jnp.float32)
            + keep_inv * (grad_normed - x_float * keep_inv * keep_inv * inner_term)
        ).astype(jnp.bfloat16)
        mine = section_now == k
        keep_upstream = jnp.where(mine, upstream, keep_upstream)
        keep_grad_hidden = jnp.where(mine, grad_hidden, keep_grad_hidden)
        if k > 0:
            sent = lax.all_to_all(
                grad_rows.reshape(micro_count, batch_rows, feature_count), "peer", 1, 1, tiled=True
            )
            moved = lax.ppermute(sent, "section", [(k, k - 1)])
            upstream = permute_rows(send_onehot[k - 1], moved, "mdq,mdf->mqf").reshape(
                row_count, feature_count
            )

    bits_count = peer_count.bit_length() - 1
    peers = jnp.arange(peer_count, dtype=jnp.int32)
    order_even = [1, 4, 2, 5, 3][: bits_count - 1]
    order_odd = [4, 1, 5, 2, 3][: bits_count - 1]
    position_core = peers >> (bits_count - 1)
    position_peer = position_core
    for t in range(bits_count - 1):
        chosen = jnp.where(position_core == 0, order_even[t], order_odd[t])
        position_peer = position_peer + (((peers >> (bits_count - 2 - t)) & 1) << chosen)
    bit_table = jnp.right_shift(position_peer[:, None], bit_order[None, :]) & 1
    weights = jnp.left_shift(jnp.int32(1), bits_count - 1 - jnp.arange(bits_count, dtype=jnp.int32))
    source_chunk = jnp.sum(bit_table * weights[None, :], axis=1).astype(jnp.int32)
    units = down_proj.shape[0]
    chunk_rows = 2 * units // peer_count
    column_source = (
        source_chunk[:, None] * chunk_rows + jnp.arange(chunk_rows, dtype=jnp.int32)[None, :]
    ).reshape(-1)
    left = jnp.zeros((2 * row_count, 2 * units), jnp.bfloat16)
    left = left.at[:row_count, :units].set(keep_grad_hidden).at[row_count:, units:].set(keep_active)
    left = jnp.take(left, column_source, axis=1)
    right = jnp.concatenate([keep_normed, keep_upstream], axis=0)
    current = contract_first(left, right)
    core_now = peer_now & 1
    stage_bits = [(0, 0)] + list(zip(order_even, order_odd))
    for even_bit, odd_bit in stage_bits:
        bit_now = jnp.where(core_now == 0, even_bit, odd_bit)
        own_bit = (peer_now >> bit_now) & 1
        half_len = current.shape[0] // 2
        outgoing = lax.dynamic_slice_in_dim(current, (1 - own_bit) * half_len, half_len, axis=0)
        kept = lax.dynamic_slice_in_dim(current, own_bit * half_len, half_len, axis=0)
        pairs = [
            (source, source ^ (1 << (even_bit if source % 2 == 0 else odd_bit)))
            for source in range(peer_count)
        ]
        arrived = lax.ppermute(outgoing.astype(jnp.bfloat16), "peer", pairs)
        current = kept + arrived.astype(jnp.float32)
    return (current * (1.0 / peer_count)).reshape(1, -1)


def solution(mesh):
    placed = (
        P("peer", None),
        P("section", None),
        P("section", "peer", None, None),
        P("section", "peer", None, None),
        P(),
        P(),
    )
    return jax.shard_map(
        local, mesh=mesh, in_specs=placed, out_specs=P("section", "peer"), check_vma=False
    )
```

```python
import jax
import jax.numpy as jnp
from jax import lax
from jax.sharding import PartitionSpec as P

gelu_scale = 0.7978845608028654
gelu_cubic = 0.044715
norm_eps = 1e-05


def gelu_parts(hidden):
    tangent = jnp.tanh(gelu_scale * (hidden + gelu_cubic * hidden * hidden * hidden))
    gelu_value = 0.5 * hidden * (1.0 + tangent)
    gelu_slope = 0.5 * (1.0 + tangent) + 0.5 * hidden * (1.0 - tangent * tangent) * gelu_scale * (
        1.0 + 3.0 * gelu_cubic * hidden * hidden
    )
    return (gelu_value, gelu_slope)


def normalize(row_block, gain_row):
    x_float = row_block.astype(jnp.float32)
    inv_rms = lax.rsqrt(jnp.mean(x_float * x_float, axis=-1, keepdims=True) + norm_eps)
    normed = (x_float * inv_rms * gain_row.astype(jnp.float32)).astype(jnp.bfloat16)
    return (x_float, inv_rms, normed)


def contract_last(left, right):
    return lax.dot_general(
        left, right, (((1,), (1,)), ((), ())), preferred_element_type=jnp.float32
    )


def contract_first(left, right):
    return lax.dot_general(
        left, right, (((0,), (0,)), ((), ())), preferred_element_type=jnp.float32
    )


def permute_rows(onehot, rows, spec):
    return jnp.einsum(spec, onehot, rows, preferred_element_type=jnp.float32).astype(rows.dtype)


def local(inputs, norm_gain, w_down, w_up, routes, bit_order):
    sections = lax.axis_size("section")
    peer_count = lax.axis_size("peer")
    section_now = lax.axis_index("section")
    peer_now = lax.axis_index("peer")
    down_proj = w_down[0, 0]
    up_proj = w_up[0, 0]
    gain_row = norm_gain[0]
    gain_float = gain_row.astype(jnp.float32)
    micro_count = routes.shape[1]
    batch_rows = routes.shape[3]
    feature_count = inputs.shape[1]
    row_count = micro_count * batch_rows

    slots = jnp.arange(batch_rows, dtype=jnp.int32)
    own_lanes = routes[:, :, peer_now, :]
    arrived_rows = (peer_now - slots) % batch_rows
    slot_lanes = jnp.concatenate(
        [own_lanes[:1], jnp.take(own_lanes[1:], arrived_rows, axis=2)], axis=0
    )
    destinations = (peer_now + slot_lanes) % peer_count
    send_onehot = (
        destinations[:, :, None, :] == jnp.arange(peer_count, dtype=jnp.int32)[None, None, :, None]
    ).astype(jnp.bfloat16)

    pieces = inputs.reshape(micro_count, batch_rows, feature_count)
    xs = [pieces[m] for m in range(micro_count)]
    units = down_proj.shape[0]
    keep_x = [jnp.zeros((batch_rows, feature_count), jnp.bfloat16) for m in range(micro_count)]
    keep_inv = [jnp.zeros((batch_rows, 1), jnp.float32) for m in range(micro_count)]
    keep_normed = [jnp.zeros((batch_rows, feature_count), jnp.bfloat16) for m in range(micro_count)]
    keep_active = [jnp.zeros((batch_rows, units), jnp.bfloat16) for m in range(micro_count)]
    keep_slope = [jnp.zeros((batch_rows, units), jnp.float32) for m in range(micro_count)]
    upstreams = [None] * micro_count
    for k in range(sections):
        mine = section_now == k
        for m in range(micro_count):
            flat = xs[m]
            x_float, inv_rms, normed = normalize(flat, gain_row)
            hidden = contract_last(normed, down_proj)
            gelu_value, gelu_slope = gelu_parts(hidden)
            active = gelu_value.astype(jnp.bfloat16)
            outputs = (
                x_float + jnp.dot(active, up_proj, preferred_element_type=jnp.float32)
            ).astype(jnp.bfloat16)
            keep_x[m] = jnp.where(mine, flat, keep_x[m])
            keep_inv[m] = jnp.where(mine, inv_rms, keep_inv[m])
            keep_normed[m] = jnp.where(mine, normed, keep_normed[m])
            keep_active[m] = jnp.where(mine, active, keep_active[m])
            keep_slope[m] = jnp.where(mine, gelu_slope, keep_slope[m])
            if k < sections - 1:
                packed = permute_rows(send_onehot[k, m], outputs, "dq,qf->df")
                received = lax.all_to_all(packed, "peer", 0, 0, tiled=True)
                xs[m] = lax.ppermute(received, "section", [(k, k + 1)])
            else:
                upstreams[m] = outputs

    keep_upstream = [jnp.zeros((batch_rows, feature_count), jnp.bfloat16) for m in range(micro_count)]
    keep_grad_hidden = [jnp.zeros((batch_rows, units), jnp.bfloat16) for m in range(micro_count)]
    for k in reversed(range(sections)):
        mine = section_now == k
        for m in range(micro_count):
            upstream = upstreams[m]
            x_float = keep_x[m].astype(jnp.float32)
            inv_rms = keep_inv[m]
            grad_active = contract_last(upstream, up_proj)
            grad_hidden = (grad_active * keep_slope[m]).astype(jnp.bfloat16)
            grad_normed = (
                jnp.dot(grad_hidden, down_proj, preferred_element_type=jnp.float32) * gain_float
            )
            inner_term = jnp.mean(grad_normed * x_float, axis=-1, keepdims=True)
            grad_rows = (
                upstream.astype(jnp.float32)
                + inv_rms * (grad_normed - x_float * inv_rms * inv_rms * inner_term)
            ).astype(jnp.bfloat16)
            keep_upstream[m] = jnp.where(mine, upstream, keep_upstream[m])
            keep_grad_hidden[m] = jnp.where(mine, grad_hidden, keep_grad_hidden[m])
            if k > 0:
                sent = lax.all_to_all(grad_rows, "peer", 0, 0, tiled=True)
                moved = lax.ppermute(sent, "section", [(k, k - 1)])
                upstreams[m] = permute_rows(send_onehot[k - 1, m], moved, "dq,df->qf")

    keep_grad_hidden = jnp.concatenate(keep_grad_hidden, axis=0)
    keep_active = jnp.concatenate(keep_active, axis=0)
    keep_normed = jnp.concatenate(keep_normed, axis=0)
    keep_upstream = jnp.concatenate(keep_upstream, axis=0)

    bits_count = peer_count.bit_length() - 1
    peers = jnp.arange(peer_count, dtype=jnp.int32)
    order_even = [1, 4, 2, 5, 3][: bits_count - 1]
    order_odd = [4, 1, 5, 2, 3][: bits_count - 1]
    position_core = peers >> (bits_count - 1)
    position_peer = position_core
    for t in range(bits_count - 1):
        chosen = jnp.where(position_core == 0, order_even[t], order_odd[t])
        position_peer = position_peer + (((peers >> (bits_count - 2 - t)) & 1) << chosen)
    bit_table = jnp.right_shift(position_peer[:, None], bit_order[None, :]) & 1
    weights = jnp.left_shift(jnp.int32(1), bits_count - 1 - jnp.arange(bits_count, dtype=jnp.int32))
    source_chunk = jnp.sum(bit_table * weights[None, :], axis=1).astype(jnp.int32)
    units = down_proj.shape[0]
    chunk_rows = 2 * units // peer_count
    column_source = (
        source_chunk[:, None] * chunk_rows + jnp.arange(chunk_rows, dtype=jnp.int32)[None, :]
    ).reshape(-1)
    left = jnp.zeros((2 * row_count, 2 * units), jnp.bfloat16)
    left = left.at[:row_count, :units].set(keep_grad_hidden).at[row_count:, units:].set(keep_active)
    left = jnp.take(left, column_source, axis=1)
    right = jnp.concatenate([keep_normed, keep_upstream], axis=0)
    current = contract_first(left, right)
    core_now = peer_now & 1
    stage_bits = [(0, 0)] + list(zip(order_even, order_odd))
    for even_bit, odd_bit in stage_bits:
        bit_now = jnp.where(core_now == 0, even_bit, odd_bit)
        own_bit = (peer_now >> bit_now) & 1
        half_len = current.shape[0] // 2
        outgoing = lax.dynamic_slice_in_dim(current, (1 - own_bit) * half_len, half_len, axis=0)
        kept = lax.dynamic_slice_in_dim(current, own_bit * half_len, half_len, axis=0)
        pairs = [
            (source, source ^ (1 << (even_bit if source % 2 == 0 else odd_bit)))
            for source in range(peer_count)
        ]
        arrived = lax.ppermute(outgoing.astype(jnp.bfloat16), "peer", pairs)
        current = kept + arrived.astype(jnp.float32)
    return (current * (1.0 / peer_count)).reshape(1, -1)


def solution(mesh):
    placed = (
        P("peer", None),
        P("section", None),
        P("section", "peer", None, None),
        P("section", "peer", None, None),
        P(),
        P(),
    )
    return jax.shard_map(
        local, mesh=mesh, in_specs=placed, out_specs=P("section", "peer"), check_vma=False
    )
```

```python
import jax
import jax.numpy as jnp
from jax import lax
from jax.sharding import PartitionSpec as P

gelu_scale = 0.7978845608028654
gelu_cubic = 0.044715
norm_eps = 1e-05


def gelu_parts(hidden):
    tangent = jnp.tanh(gelu_scale * (hidden + gelu_cubic * hidden * hidden * hidden))
    gelu_value = 0.5 * hidden * (1.0 + tangent)
    gelu_slope = 0.5 * (1.0 + tangent) + 0.5 * hidden * (1.0 - tangent * tangent) * gelu_scale * (
        1.0 + 3.0 * gelu_cubic * hidden * hidden
    )
    return (gelu_value, gelu_slope)


def normalize(row_block, gain_row):
    x_float = row_block.astype(jnp.float32)
    inv_rms = lax.rsqrt(jnp.mean(x_float * x_float, axis=-1, keepdims=True) + norm_eps)
    normed = (x_float * inv_rms * gain_row.astype(jnp.float32)).astype(jnp.bfloat16)
    return (x_float, inv_rms, normed)


def contract_last(left, right):
    return lax.dot_general(
        left, right, (((1,), (1,)), ((), ())), preferred_element_type=jnp.float32
    )


def contract_first(left, right):
    return lax.dot_general(
        left, right, (((0,), (0,)), ((), ())), preferred_element_type=jnp.float32
    )


def permute_rows(onehot, rows, spec):
    return jnp.einsum(spec, onehot, rows, preferred_element_type=jnp.float32).astype(rows.dtype)


def local(inputs, norm_gain, w_down, w_up, routes, bit_order):
    sections = lax.axis_size("section")
    peer_count = lax.axis_size("peer")
    section_now = lax.axis_index("section")
    peer_now = lax.axis_index("peer")
    down_proj = w_down[0, 0]
    up_proj = w_up[0, 0]
    gain_row = norm_gain[0]
    gain_float = gain_row.astype(jnp.float32)
    micro_count = routes.shape[1]
    batch_rows = routes.shape[3]
    feature_count = inputs.shape[1]
    row_count = micro_count * batch_rows

    slots = jnp.arange(batch_rows, dtype=jnp.int32)
    own_lanes = routes[:, :, peer_now, :]
    arrived_rows = (peer_now - slots) % batch_rows
    slot_lanes = jnp.concatenate(
        [own_lanes[:1], jnp.take(own_lanes[1:], arrived_rows, axis=2)], axis=0
    )
    destinations = (peer_now + slot_lanes) % peer_count
    send_onehot = (
        destinations[:, :, None, :] == jnp.arange(peer_count, dtype=jnp.int32)[None, None, :, None]
    ).astype(jnp.bfloat16)

    x = inputs.reshape(micro_count, batch_rows, feature_count)
    keep_x = jnp.zeros((row_count, feature_count), jnp.bfloat16)
    keep_inv = jnp.zeros((row_count, 1), jnp.float32)
    keep_normed = jnp.zeros((row_count, feature_count), jnp.bfloat16)
    keep_active = jnp.zeros((row_count, down_proj.shape[0]), jnp.bfloat16)
    keep_slope = jnp.zeros((row_count, down_proj.shape[0]), jnp.float32)
    upstream = None
    for k in range(sections):
        flat = x.reshape(row_count, feature_count)
        x_float, inv_rms, normed = normalize(flat, gain_row)
        hidden = contract_last(normed, down_proj)
        gelu_value, gelu_slope = gelu_parts(hidden)
        active = gelu_value.astype(jnp.bfloat16)
        outputs = (x_float + jnp.dot(active, up_proj, preferred_element_type=jnp.float32)).astype(
            jnp.bfloat16
        )
        mine = section_now == k
        keep_x = jnp.where(mine, flat, keep_x)
        keep_inv = jnp.where(mine, inv_rms, keep_inv)
        keep_normed = jnp.where(mine, normed, keep_normed)
        keep_active = jnp.where(mine, active, keep_active)
        keep_slope = jnp.where(mine, gelu_slope, keep_slope)
        if k < sections - 1:
            blocks = outputs.reshape(micro_count, batch_rows, feature_count)
            half = feature_count // 2
            raw_later = lax.ppermute(blocks[:, :, half:], "section", [(k, k + 1)])
            packed = permute_rows(send_onehot[k], blocks[:, :, :half], "mdq,mqf->mdf")
            received = lax.all_to_all(packed, "peer", 1, 1, tiled=True)
            moved = lax.ppermute(received, "section", [(k, k + 1)])
            packed_later = permute_rows(send_onehot[k], raw_later, "mdq,mqf->mdf")
            received_later = lax.all_to_all(packed_later, "peer", 1, 1, tiled=True)
            x = jnp.concatenate([moved, received_later], axis=2)
        else:
            upstream = outputs

    x_float = keep_x.astype(jnp.float32)
    keep_upstream = jnp.zeros((row_count, feature_count), jnp.bfloat16)
    keep_grad_hidden = jnp.zeros((row_count, down_proj.shape[0]), jnp.bfloat16)
    for k in reversed(range(sections)):
        grad_active = contract_last(upstream, up_proj)
        grad_hidden = (grad_active * keep_slope).astype(jnp.bfloat16)
        grad_normed = jnp.dot(grad_hidden, down_proj, preferred_element_type=jnp.float32) * gain_float
        inner_term = jnp.mean(grad_normed * x_float, axis=-1, keepdims=True)
        grad_rows = (
            upstream.astype(jnp.float32)
            + keep_inv * (grad_normed - x_float * keep_inv * keep_inv * inner_term)
        ).astype(jnp.bfloat16)
        mine = section_now == k
        keep_upstream = jnp.where(mine, upstream, keep_upstream)
        keep_grad_hidden = jnp.where(mine, grad_hidden, keep_grad_hidden)
        if k > 0:
            blocks = grad_rows.reshape(micro_count, batch_rows, feature_count)
            half = feature_count // 2
            raw_later = lax.ppermute(blocks[:, :, half:], "section", [(k, k - 1)])
            sent = lax.all_to_all(blocks[:, :, :half], "peer", 1, 1, tiled=True)
            moved = lax.ppermute(sent, "section", [(k, k - 1)])
            sent_later = lax.all_to_all(raw_later, "peer", 1, 1, tiled=True)
            upstream = permute_rows(
                send_onehot[k - 1], jnp.concatenate([moved, sent_later], axis=2), "mdq,mdf->mqf"
            ).reshape(row_count, feature_count)

    bits_count = peer_count.bit_length() - 1
    peers = jnp.arange(peer_count, dtype=jnp.int32)
    order_even = [1, 4, 2, 5, 3][: bits_count - 1]
    order_odd = [4, 1, 5, 2, 3][: bits_count - 1]
    position_core = peers >> (bits_count - 1)
    position_peer = position_core
    for t in range(bits_count - 1):
        chosen = jnp.where(position_core == 0, order_even[t], order_odd[t])
        position_peer = position_peer + (((peers >> (bits_count - 2 - t)) & 1) << chosen)
    bit_table = jnp.right_shift(position_peer[:, None], bit_order[None, :]) & 1
    weights = jnp.left_shift(jnp.int32(1), bits_count - 1 - jnp.arange(bits_count, dtype=jnp.int32))
    source_chunk = jnp.sum(bit_table * weights[None, :], axis=1).astype(jnp.int32)
    units = down_proj.shape[0]
    chunk_rows = 2 * units // peer_count
    column_source = (
        source_chunk[:, None] * chunk_rows + jnp.arange(chunk_rows, dtype=jnp.int32)[None, :]
    ).reshape(-1)
    left = jnp.zeros((2 * row_count, 2 * units), jnp.bfloat16)
    left = left.at[:row_count, :units].set(keep_grad_hidden).at[row_count:, units:].set(keep_active)
    left = jnp.take(left, column_source, axis=1)
    right = jnp.concatenate([keep_normed, keep_upstream], axis=0)
    current = contract_first(left, right)
    core_now = peer_now & 1
    stage_bits = [(0, 0)] + list(zip(order_even, order_odd))
    for even_bit, odd_bit in stage_bits:
        bit_now = jnp.where(core_now == 0, even_bit, odd_bit)
        own_bit = (peer_now >> bit_now) & 1
        half_len = current.shape[0] // 2
        outgoing = lax.dynamic_slice_in_dim(current, (1 - own_bit) * half_len, half_len, axis=0)
        kept = lax.dynamic_slice_in_dim(current, own_bit * half_len, half_len, axis=0)
        pairs = [
            (source, source ^ (1 << (even_bit if source % 2 == 0 else odd_bit)))
            for source in range(peer_count)
        ]
        arrived = lax.ppermute(outgoing.astype(jnp.bfloat16), "peer", pairs)
        current = kept + arrived.astype(jnp.float32)
    return (current * (1.0 / peer_count)).reshape(1, -1)


def solution(mesh):
    placed = (
        P("peer", None),
        P("section", None),
        P("section", "peer", None, None),
        P("section", "peer", None, None),
        P(),
        P(),
    )
    return jax.shard_map(
        local, mesh=mesh, in_specs=placed, out_specs=P("section", "peer"), check_vma=False
    )
```

```python
import jax
import jax.numpy as jnp
from jax import lax
from jax.sharding import PartitionSpec as P

gelu_scale = 0.7978845608028654
gelu_cubic = 0.044715
norm_eps = 1e-05


def gelu_parts(hidden):
    tangent = jnp.tanh(gelu_scale * (hidden + gelu_cubic * hidden * hidden * hidden))
    gelu_value = 0.5 * hidden * (1.0 + tangent)
    gelu_slope = 0.5 * (1.0 + tangent) + 0.5 * hidden * (1.0 - tangent * tangent) * gelu_scale * (
        1.0 + 3.0 * gelu_cubic * hidden * hidden
    )
    return (gelu_value, gelu_slope)


def normalize(row_block, gain_row):
    x_float = row_block.astype(jnp.float32)
    inv_rms = lax.rsqrt(jnp.mean(x_float * x_float, axis=-1, keepdims=True) + norm_eps)
    normed = (x_float * inv_rms * gain_row.astype(jnp.float32)).astype(jnp.bfloat16)
    return (x_float, inv_rms, normed)


def contract_last(left, right):
    return lax.dot_general(
        left, right, (((1,), (1,)), ((), ())), preferred_element_type=jnp.float32
    )


def contract_first(left, right):
    return lax.dot_general(
        left, right, (((0,), (0,)), ((), ())), preferred_element_type=jnp.float32
    )


def permute_rows(onehot, rows, spec):
    return jnp.einsum(spec, onehot, rows, preferred_element_type=jnp.float32).astype(rows.dtype)


def local(inputs, norm_gain, w_down, w_up, routes, bit_order):
    sections = lax.axis_size("section")
    peer_count = lax.axis_size("peer")
    section_now = lax.axis_index("section")
    peer_now = lax.axis_index("peer")
    down_proj = w_down[0, 0]
    up_proj = w_up[0, 0]
    gain_row = norm_gain[0]
    gain_float = gain_row.astype(jnp.float32)
    micro_count = routes.shape[1]
    batch_rows = routes.shape[3]
    feature_count = inputs.shape[1]
    row_count = micro_count * batch_rows

    slots = jnp.arange(batch_rows, dtype=jnp.int32)
    own_lanes = routes[:, :, peer_now, :]
    arrived_rows = (peer_now - slots) % batch_rows
    slot_lanes = jnp.concatenate(
        [own_lanes[:1], jnp.take(own_lanes[1:], arrived_rows, axis=2)], axis=0
    )
    destinations = (peer_now + slot_lanes) % peer_count
    send_onehot = (
        destinations[:, :, None, :] == jnp.arange(peer_count, dtype=jnp.int32)[None, None, :, None]
    ).astype(jnp.bfloat16)

    units = down_proj.shape[0]

    def forward_layer(flat):
        x_float, inv_rms, normed = normalize(flat, gain_row)
        hidden = contract_last(normed, down_proj)
        gelu_value, gelu_slope = gelu_parts(hidden)
        active = gelu_value.astype(jnp.bfloat16)
        outputs = (x_float + jnp.dot(active, up_proj, preferred_element_type=jnp.float32)).astype(
            jnp.bfloat16
        )
        return (inv_rms, normed, active, gelu_slope, outputs)

    forward_pairs = [(j, j + 1) for j in range(sections - 1)]

    def forward_step(k, carry):
        flat, keep_x, keep_inv, keep_normed, keep_active, keep_slope = carry
        inv_rms, normed, active, gelu_slope, outputs = forward_layer(flat)
        mine = section_now == k
        keep_x = jnp.where(mine, flat, keep_x)
        keep_inv = jnp.where(mine, inv_rms, keep_inv)
        keep_normed = jnp.where(mine, normed, keep_normed)
        keep_active = jnp.where(mine, active, keep_active)
        keep_slope = jnp.where(mine, gelu_slope, keep_slope)
        packed = permute_rows(
            send_onehot[k], outputs.reshape(micro_count, batch_rows, feature_count), "mdq,mqf->mdf"
        )
        received = lax.all_to_all(packed, "peer", 1, 1, tiled=True)
        moved = lax.ppermute(received, "section", forward_pairs)
        return (moved.reshape(row_count, feature_count), keep_x, keep_inv, keep_normed, keep_active, keep_slope)

    carry = (
        inputs,
        jnp.zeros((row_count, feature_count), jnp.bfloat16),
        jnp.zeros((row_count, 1), jnp.float32),
        jnp.zeros((row_count, feature_count), jnp.bfloat16),
        jnp.zeros((row_count, units), jnp.bfloat16),
        jnp.zeros((row_count, units), jnp.float32),
    )
    flat, keep_x, keep_inv, keep_normed, keep_active, keep_slope = lax.fori_loop(
        0, sections - 1, forward_step, carry
    )
    inv_rms, normed, active, gelu_slope, upstream = forward_layer(flat)
    mine = section_now == sections - 1
    keep_x = jnp.where(mine, flat, keep_x)
    keep_inv = jnp.where(mine, inv_rms, keep_inv)
    keep_normed = jnp.where(mine, normed, keep_normed)
    keep_active = jnp.where(mine, active, keep_active)
    keep_slope = jnp.where(mine, gelu_slope, keep_slope)

    x_float = keep_x.astype(jnp.float32)

    def backward_layer(upstream):
        grad_active = contract_last(upstream, up_proj)
        grad_hidden = (grad_active * keep_slope).astype(jnp.bfloat16)
        grad_normed = jnp.dot(grad_hidden, down_proj, preferred_element_type=jnp.float32) * gain_float
        inner_term = jnp.mean(grad_normed * x_float, axis=-1, keepdims=True)
        grad_rows = (
            upstream.astype(jnp.float32)
            + keep_inv * (grad_normed - x_float * keep_inv * keep_inv * inner_term)
        ).astype(jnp.bfloat16)
        return (grad_hidden, grad_rows)

    backward_pairs = [(j + 1, j) for j in range(sections - 1)]

    def backward_step(t, carry):
        upstream, keep_upstream, keep_grad_hidden = carry
        k = sections - 1 - t
        grad_hidden, grad_rows = backward_layer(upstream)
        mine = section_now == k
        keep_upstream = jnp.where(mine, upstream, keep_upstream)
        keep_grad_hidden = jnp.where(mine, grad_hidden, keep_grad_hidden)
        sent = lax.all_to_all(
            grad_rows.reshape(micro_count, batch_rows, feature_count), "peer", 1, 1, tiled=True
        )
        moved = lax.ppermute(sent, "section", backward_pairs)
        upstream = permute_rows(send_onehot[k - 1], moved, "mdq,mdf->mqf").reshape(
            row_count, feature_count
        )
        return (upstream, keep_upstream, keep_grad_hidden)

    carry = (
        upstream,
        jnp.zeros((row_count, feature_count), jnp.bfloat16),
        jnp.zeros((row_count, units), jnp.bfloat16),
    )
    upstream, keep_upstream, keep_grad_hidden = lax.fori_loop(0, sections - 1, backward_step, carry)
    grad_hidden, grad_rows = backward_layer(upstream)
    mine = section_now == 0
    keep_upstream = jnp.where(mine, upstream, keep_upstream)
    keep_grad_hidden = jnp.where(mine, grad_hidden, keep_grad_hidden)

    bits_count = peer_count.bit_length() - 1
    peers = jnp.arange(peer_count, dtype=jnp.int32)
    order_even = [1, 4, 2, 5, 3][: bits_count - 1]
    order_odd = [4, 1, 5, 2, 3][: bits_count - 1]
    position_core = peers >> (bits_count - 1)
    position_peer = position_core
    for t in range(bits_count - 1):
        chosen = jnp.where(position_core == 0, order_even[t], order_odd[t])
        position_peer = position_peer + (((peers >> (bits_count - 2 - t)) & 1) << chosen)
    bit_table = jnp.right_shift(position_peer[:, None], bit_order[None, :]) & 1
    weights = jnp.left_shift(jnp.int32(1), bits_count - 1 - jnp.arange(bits_count, dtype=jnp.int32))
    source_chunk = jnp.sum(bit_table * weights[None, :], axis=1).astype(jnp.int32)
    units = down_proj.shape[0]
    chunk_rows = 2 * units // peer_count
    column_source = (
        source_chunk[:, None] * chunk_rows + jnp.arange(chunk_rows, dtype=jnp.int32)[None, :]
    ).reshape(-1)
    left = jnp.zeros((2 * row_count, 2 * units), jnp.bfloat16)
    left = left.at[:row_count, :units].set(keep_grad_hidden).at[row_count:, units:].set(keep_active)
    left = jnp.take(left, column_source, axis=1)
    right = jnp.concatenate([keep_normed, keep_upstream], axis=0)
    current = contract_first(left, right)
    core_now = peer_now & 1
    stage_bits = [(0, 0)] + list(zip(order_even, order_odd))
    for even_bit, odd_bit in stage_bits:
        bit_now = jnp.where(core_now == 0, even_bit, odd_bit)
        own_bit = (peer_now >> bit_now) & 1
        half_len = current.shape[0] // 2
        outgoing = lax.dynamic_slice_in_dim(current, (1 - own_bit) * half_len, half_len, axis=0)
        kept = lax.dynamic_slice_in_dim(current, own_bit * half_len, half_len, axis=0)
        pairs = [
            (source, source ^ (1 << (even_bit if source % 2 == 0 else odd_bit)))
            for source in range(peer_count)
        ]
        arrived = lax.ppermute(outgoing.astype(jnp.bfloat16), "peer", pairs)
        current = kept + arrived.astype(jnp.float32)
    return (current * (1.0 / peer_count)).reshape(1, -1)


def solution(mesh):
    placed = (
        P("peer", None),
        P("section", None),
        P("section", "peer", None, None),
        P("section", "peer", None, None),
        P(),
        P(),
    )
    return jax.shard_map(
        local, mesh=mesh, in_specs=placed, out_specs=P("section", "peer"), check_vma=False
    )
```

```python
import jax
import jax.numpy as jnp
from jax import lax
from jax.sharding import PartitionSpec as P

gelu_scale = 0.7978845608028654
gelu_cubic = 0.044715
norm_eps = 1e-05


def gelu_parts(hidden):
    tangent = jnp.tanh(gelu_scale * (hidden + gelu_cubic * hidden * hidden * hidden))
    gelu_value = 0.5 * hidden * (1.0 + tangent)
    gelu_slope = 0.5 * (1.0 + tangent) + 0.5 * hidden * (1.0 - tangent * tangent) * gelu_scale * (
        1.0 + 3.0 * gelu_cubic * hidden * hidden
    )
    return (gelu_value, gelu_slope)


def normalize(row_block, gain_row):
    x_float = row_block.astype(jnp.float32)
    inv_rms = lax.rsqrt(jnp.mean(x_float * x_float, axis=-1, keepdims=True) + norm_eps)
    normed = (x_float * inv_rms * gain_row.astype(jnp.float32)).astype(jnp.bfloat16)
    return (x_float, inv_rms, normed)


def contract_last(left, right):
    return lax.dot_general(
        left, right, (((1,), (1,)), ((), ())), preferred_element_type=jnp.float32
    )


def contract_first(left, right):
    return lax.dot_general(
        left, right, (((0,), (0,)), ((), ())), preferred_element_type=jnp.float32
    )


def permute_rows(onehot, rows, spec):
    return jnp.einsum(spec, onehot, rows, preferred_element_type=jnp.float32).astype(rows.dtype)


def local(inputs, norm_gain, w_down, w_up, routes, bit_order):
    sections = lax.axis_size("section")
    peer_count = lax.axis_size("peer")
    section_now = lax.axis_index("section")
    peer_now = lax.axis_index("peer")
    down_proj = w_down[0, 0]
    up_proj = w_up[0, 0]
    gain_row = norm_gain[0]
    gain_float = gain_row.astype(jnp.float32)
    micro_count = routes.shape[1]
    batch_rows = routes.shape[3]
    feature_count = inputs.shape[1]
    row_count = micro_count * batch_rows

    slots = jnp.arange(batch_rows, dtype=jnp.int32)
    own_lanes = routes[:, :, peer_now, :]
    arrived_rows = (peer_now - slots) % batch_rows
    slot_lanes = jnp.concatenate(
        [own_lanes[:1], jnp.take(own_lanes[1:], arrived_rows, axis=2)], axis=0
    )
    destinations = (peer_now + slot_lanes) % peer_count
    send_onehot = (
        destinations[:, :, None, :] == jnp.arange(peer_count, dtype=jnp.int32)[None, None, :, None]
    ).astype(jnp.bfloat16)

    x = inputs.reshape(micro_count, batch_rows, feature_count)
    keep_x = jnp.zeros((row_count, feature_count), jnp.bfloat16)
    upstream = None
    for k in range(sections):
        flat = x.reshape(row_count, feature_count)
        x_float, inv_rms, normed = normalize(flat, gain_row)
        hidden = contract_last(normed, down_proj)
        gelu_value, gelu_slope = gelu_parts(hidden)
        active = gelu_value.astype(jnp.bfloat16)
        outputs = (x_float + jnp.dot(active, up_proj, preferred_element_type=jnp.float32)).astype(
            jnp.bfloat16
        )
        keep_x = jnp.where(section_now == k, flat, keep_x)
        if k < sections - 1:
            packed = permute_rows(
                send_onehot[k], outputs.reshape(micro_count, batch_rows, feature_count), "mdq,mqf->mdf"
            )
            received = lax.all_to_all(packed, "peer", 1, 1, tiled=True)
            x = lax.ppermute(received, "section", [(k, k + 1)])
        else:
            upstream = outputs

    x_float, keep_inv, keep_normed = normalize(keep_x, gain_row)
    gelu_value, keep_slope = gelu_parts(contract_last(keep_normed, down_proj))
    keep_active = gelu_value.astype(jnp.bfloat16)
    keep_upstream = jnp.zeros((row_count, feature_count), jnp.bfloat16)
    keep_grad_hidden = jnp.zeros((row_count, down_proj.shape[0]), jnp.bfloat16)
    for k in reversed(range(sections)):
        grad_active = contract_last(upstream, up_proj)
        grad_hidden = (grad_active * keep_slope).astype(jnp.bfloat16)
        grad_normed = jnp.dot(grad_hidden, down_proj, preferred_element_type=jnp.float32) * gain_float
        inner_term = jnp.mean(grad_normed * x_float, axis=-1, keepdims=True)
        grad_rows = (
            upstream.astype(jnp.float32)
            + keep_inv * (grad_normed - x_float * keep_inv * keep_inv * inner_term)
        ).astype(jnp.bfloat16)
        mine = section_now == k
        keep_upstream = jnp.where(mine, upstream, keep_upstream)
        keep_grad_hidden = jnp.where(mine, grad_hidden, keep_grad_hidden)
        if k > 0:
            sent = lax.all_to_all(
                grad_rows.reshape(micro_count, batch_rows, feature_count), "peer", 1, 1, tiled=True
            )
            moved = lax.ppermute(sent, "section", [(k, k - 1)])
            upstream = permute_rows(send_onehot[k - 1], moved, "mdq,mdf->mqf").reshape(
                row_count, feature_count
            )

    bits_count = peer_count.bit_length() - 1
    peers = jnp.arange(peer_count, dtype=jnp.int32)
    order_even = [1, 4, 2, 5, 3][: bits_count - 1]
    order_odd = [4, 1, 5, 2, 3][: bits_count - 1]
    position_core = peers >> (bits_count - 1)
    position_peer = position_core
    for t in range(bits_count - 1):
        chosen = jnp.where(position_core == 0, order_even[t], order_odd[t])
        position_peer = position_peer + (((peers >> (bits_count - 2 - t)) & 1) << chosen)
    bit_table = jnp.right_shift(position_peer[:, None], bit_order[None, :]) & 1
    weights = jnp.left_shift(jnp.int32(1), bits_count - 1 - jnp.arange(bits_count, dtype=jnp.int32))
    source_chunk = jnp.sum(bit_table * weights[None, :], axis=1).astype(jnp.int32)
    units = down_proj.shape[0]
    chunk_rows = 2 * units // peer_count
    column_source = (
        source_chunk[:, None] * chunk_rows + jnp.arange(chunk_rows, dtype=jnp.int32)[None, :]
    ).reshape(-1)
    left = jnp.zeros((2 * row_count, 2 * units), jnp.bfloat16)
    left = left.at[:row_count, :units].set(keep_grad_hidden).at[row_count:, units:].set(keep_active)
    left = jnp.take(left, column_source, axis=1)
    right = jnp.concatenate([keep_normed, keep_upstream], axis=0)
    current = contract_first(left, right)
    core_now = peer_now & 1
    stage_bits = [(0, 0)] + list(zip(order_even, order_odd))
    for even_bit, odd_bit in stage_bits:
        bit_now = jnp.where(core_now == 0, even_bit, odd_bit)
        own_bit = (peer_now >> bit_now) & 1
        half_len = current.shape[0] // 2
        outgoing = lax.dynamic_slice_in_dim(current, (1 - own_bit) * half_len, half_len, axis=0)
        kept = lax.dynamic_slice_in_dim(current, own_bit * half_len, half_len, axis=0)
        pairs = [
            (source, source ^ (1 << (even_bit if source % 2 == 0 else odd_bit)))
            for source in range(peer_count)
        ]
        arrived = lax.ppermute(outgoing.astype(jnp.bfloat16), "peer", pairs)
        current = kept + arrived.astype(jnp.float32)
    return (current * (1.0 / peer_count)).reshape(1, -1)


def solution(mesh):
    placed = (
        P("peer", None),
        P("section", None),
        P("section", "peer", None, None),
        P("section", "peer", None, None),
        P(),
        P(),
    )
    return jax.shard_map(
        local, mesh=mesh, in_specs=placed, out_specs=P("section", "peer"), check_vma=False
    )
```
